256 devices in a mesh: cells: 16 (over z, core), tracer: 16 (over y, x).
Axes of the slice: x: 4, y: 4, z: 8, core: 2. Of those that a mesh axis runs over, the one named last changes fastest.
Arguments:
- adjoint: float32 [64, 65536], P('tracer', 'cells'), may hold values from -6 to 6
- blocks: float32 [2048, 128, 128], P('cells'), may hold values from -0.375 to 0.375
- row_ptr: int32 [16, 33], P('cells'), may hold values from 0 to 128, as said below
- col_idx: int32 [2048], P('cells'), may hold values from 0 to 511, as said below
- regime: int32 [512], P('cells'), may hold values from 0 to 7
- jac: float32 [8, 64, 64], replicated, as said below
Outputs:
- sensitivity: float32 [64, 65536], P('tracer', 'cells')
The draws below stay inside these ranges and needn't reach their ends.
Inputs may be any that keep to these rules, and one draw needn't show every extreme that they name: row_ptr[d, 0] = 0 and each block row holds 1 to 4 slots; some index of cells uses all 128 slots. `col_idx`: the first slot of each block row is its diagonal block; a live slot's column lies at most 32 blocks away from its block row, counted cyclically over the 512 blocks, and that distance is reached; slots past row_ptr[d, 32] hold any valid column. `jac`: each regime's matrix has diagonal entries of order one and off-diagonal couplings of order 0.1 between every pair of species.
All inputs are finite; a program needn't handle non-finite values.
Results may differ from the reference program's by a relative error of at most 0.0001.
Values sent between devices are 32-bit elements; how exact they have to be, the bound alone decides.
No kernel may reach another device: no remote copies, remote signals or barrier semaphores. Data moves between devices by JAX's collectives and lax.ppermute only.
A program may use at most 64 MiB of HBM per device.

```python
import math
import jax
import jax.numpy as jnp
from jax import lax

SPEC = 64
BLOCK = 128
NB_DEV = 32
KMAX = 4
STEPS = 2
NREG = 8
NNZ_DEV = 128
NB = 512
NCELL = 65536


def sparsity_pattern(key):
    base = jax.random.fold_in(key, 11)
    key_level, key_full, key_count, key_sign, key_offset = jax.random.split(base, 5)
    device_count = NB // NB_DEV
    levels = jax.random.randint(key_level, (device_count,), 2, KMAX + 1)
    full_device = jax.random.randint(key_full, (), 0, device_count)
    raw_counts = jax.random.randint(key_count, (device_count, NB_DEV), 0, 1 << 20)
    row_counts = raw_counts % levels[:, None] + 1
    row_counts = jnp.where(jnp.arange(device_count)[:, None] == full_device, KMAX, row_counts)
    pointers = jnp.concatenate([jnp.zeros((device_count, 1), jnp.int32), jnp.cumsum(row_counts, axis=1).astype(jnp.int32)], axis=1)
    slot_ids = jnp.arange(NNZ_DEV).astype(jnp.int32)
    local_rows = jnp.sum((pointers[:, 1:, None] <= slot_ids[None, None, :]).astype(jnp.int32), axis=1)
    local_rows = jnp.minimum(local_rows, NB_DEV - 1)
    starts = jnp.take_along_axis(pointers, local_rows, axis=1)
    position = slot_ids[None, :] - starts
    signs = jax.random.randint(key_sign, (device_count, NNZ_DEV), 0, 2) * 2 - 1
    offsets = jax.random.randint(key_offset, (device_count, NNZ_DEV), -NB_DEV, NB_DEV + 1)
    offsets = jnp.where(position == 0, 0, jnp.where(position == 1, signs * NB_DEV, offsets))
    columns = jnp.mod(jnp.arange(device_count)[:, None] * NB_DEV + local_rows + offsets, NB)
    return (pointers.astype(jnp.int32), columns.reshape(-1).astype(jnp.int32))


def draw_row_ptr(key, part):
    pointers, columns = sparsity_pattern(key)
    return pointers


def draw_col_idx(key, part):
    pointers, columns = sparsity_pattern(key)
    return columns


def draw_jac(key, part):
    key_diag, key_coupling = jax.random.split(jax.random.fold_in(key, 23))
    diagonal = jax.random.uniform(key_diag, (NREG, SPEC), jnp.float32, 0.6, 1.1)
    coupling = jax.random.normal(key_coupling, (NREG, SPEC, SPEC), jnp.float32) * (0.6 / math.sqrt(SPEC))
    return coupling + diagonal[:, :, None] * jnp.eye(SPEC, dtype=jnp.float32)[None, :, :]


def with_ends(values, own_key, low, top_value):
    index_at = [jax.random.randint(jax.random.fold_in(own_key, axis), (), 0, length) for axis, length in enumerate(values.shape)]
    longest = values.shape.index(max(values.shape))
    neighbour = index_at[:longest] + [(index_at[longest] + 1) % values.shape[longest]] + index_at[longest + 1:]
    return values.at[tuple(index_at)].set(low).at[tuple(neighbour)].set(top_value)


def shard_levels(stream_key, extent, cuts, low, top_value):
    gain = 1.0
    for dim, shards_of in cuts:
        steps = jax.random.uniform(jax.random.fold_in(jax.random.fold_in(stream_key, 6), dim), (shards_of,), jnp.float32, low / len(cuts), top_value / len(cuts))
        gain = gain * jnp.repeat(jnp.exp(steps), extent[dim] // shards_of).reshape((-1,) + (1,) * (len(extent) - 1 - dim))
    return gain


def normal_values(rng, extent, width, most, shards=(), kind=jnp.bfloat16):
    drawn = width * jax.random.normal(rng, extent, jnp.float32)
    if shards:
        drawn = drawn * shard_levels(rng, extent, shards, -0.22, 0.18)
    return jnp.clip(drawn, -most, most).astype(kind)


def setup_inputs(seed: int = 0) -> dict:
    key_of = jax.random.split(jax.random.key(seed), 7)
    return {
        "adjoint": normal_values(key_of[0], (SPEC, NCELL), 1.0, 6.0, ((0, 16), (1, 16)), jnp.float32),
        "blocks": normal_values(key_of[1], (NB * KMAX, BLOCK, BLOCK), (2 * BLOCK) ** -0.5, 0.375, ((0, 16),), jnp.float32),
        "row_ptr": draw_row_ptr(jax.random.fold_in(key_of[6], 71), 0),
        "col_idx": draw_col_idx(jax.random.fold_in(key_of[6], 71), 0),
        "regime": with_ends(jax.random.randint(key_of[4], (NB,), 0, NREG), jax.random.fold_in(key_of[4], 1), 0, NREG - 1).astype(jnp.int32),
        "jac": draw_jac(jax.random.fold_in(key_of[6], 71), 0),
    }


def chemistry(moved, cell_regime, jac):
    result = jnp.zeros(moved.shape, jnp.float32)
    for regime_id in range(jac.shape[0]):
        reacted = jnp.einsum('ts,tc->sc', jac[regime_id], moved, precision=lax.Precision.HIGHEST)
        result = result + jnp.where(cell_regime[None, :] == regime_id, reacted, jnp.zeros_like(reacted))
    return result


def reference(adjoint, blocks, row_ptr, col_idx, regime, jac):
    device_count = NB // NB_DEV
    slot_ids = jnp.arange(NNZ_DEV).astype(jnp.int32)
    local_rows = jnp.sum((row_ptr[:, 1:, None] <= slot_ids[None, None, :]).astype(jnp.int32), axis=1)
    occupied = slot_ids[None, :] < row_ptr[:, -1:]
    global_rows = jnp.arange(device_count).astype(jnp.int32)[:, None] * NB_DEV + local_rows
    global_rows = jnp.where(occupied, global_rows, NB).reshape(-1)
    cell_regime = jnp.repeat(regime, BLOCK)
    adjoint_field = adjoint
    for hour_step in range(STEPS):
        gathered = adjoint_field.reshape(SPEC, NB, BLOCK)[:, col_idx, :]
        products = jnp.einsum('sij,qsj->sqi', blocks, gathered, precision=lax.Precision.HIGHEST)
        summed = jax.ops.segment_sum(products, global_rows, num_segments=NB)
        moved = jnp.transpose(summed, (1, 0, 2)).reshape(SPEC, NCELL)
        adjoint_field = chemistry(moved, cell_regime, jac)
    return adjoint_field
```

```python
import jax
import jax.numpy as jnp
from jax import lax
from jax.sharding import PartitionSpec as P

BLOCK = 128
STEPS = 2


def with_halo(cells, sides, width):
    for axis, dim in sides:
        count = lax.axis_size(axis)
        head = lax.slice_in_dim(cells, 0, width, axis=dim)
        tail = lax.slice_in_dim(cells, cells.shape[dim] - width, cells.shape[dim], axis=dim)
        cells = jnp.concatenate(
            [
                lax.ppermute(tail, axis, [(i, (i + 1) % count) for i in range(count)]),
                cells,
                lax.ppermute(head, axis, [((i + 1) % count, i) for i in range(count)]),
            ],
            axis=dim,
        )
    return cells


def chemistry_local(moved, block_jac):
    spec, cells = moved.shape
    nblk = cells // BLOCK
    per_block = moved.reshape(spec, nblk, BLOCK)
    out = jnp.einsum("but,ubc->tbc", block_jac, per_block, precision=lax.Precision.HIGHEST)
    return out.reshape(spec, cells)


def body(adjoint, blocks, row_ptr, col_idx, regime, jac):
    spec_dev, cells_dev = adjoint.shape
    nb_dev = cells_dev // BLOCK
    cell_devices = lax.axis_size("cells")
    cell_index = lax.axis_index("cells")
    tracer_devices = lax.axis_size("tracer")
    tracer_index = lax.axis_index("tracer")
    nb_total = nb_dev * cell_devices
    pointers = row_ptr[0]
    slot_count = blocks.shape[0]
    slot_ids = jnp.arange(slot_count)
    member = (
        (slot_ids[None, :] >= pointers[:-1, None]) & (slot_ids[None, :] < pointers[1:, None])
    ).astype(jnp.float32)
    live_slot = slot_ids < pointers[-1]
    local_col = jnp.mod(col_idx - (cell_index - 1) * nb_dev, nb_total)
    local_col = jnp.where(live_slot, local_col, 0)
    own_blocks = nb_dev // tracer_devices
    own_regime = lax.dynamic_slice_in_dim(regime, tracer_index * own_blocks, own_blocks)
    block_jac = jnp.take(jac, own_regime, axis=0)
    adjoint_field = adjoint
    for hour_step in range(STEPS):
        extended = with_halo(adjoint_field, (("cells", 1),), cells_dev)
        extended_blocks = extended.reshape(spec_dev, 3 * nb_dev, BLOCK)
        picked = jnp.take(extended_blocks, local_col, axis=1, mode="clip")
        picked = jnp.where(live_slot[None, :, None], picked, jnp.zeros_like(picked))
        products = jnp.einsum("sij,qsj->qsi", blocks, picked, precision=lax.Precision.HIGHEST)
        moved = jnp.einsum(
            "rs,qsi->qri", member, products, precision=lax.Precision.HIGHEST
        ).reshape(spec_dev, cells_dev)
        split = lax.all_to_all(moved, "tracer", 1, 0, tiled=True)
        reacted = chemistry_local(split, block_jac)
        adjoint_field = lax.all_to_all(reacted, "tracer", 0, 1, tiled=True)
    return adjoint_field


def solution(mesh):
    return jax.shard_map(
        body,
        mesh=mesh,
        in_specs=(
            P("tracer", "cells"),
            P("cells", None, None),
            P("cells", None),
            P("cells"),
            P("cells"),
            P(),
        ),
        out_specs=P("tracer", "cells"),
        check_vma=False,
    )
```

```python
import jax
import jax.numpy as jnp
from jax import lax
from jax.experimental import pallas as pl
from jax.experimental.pallas import tpu as pltpu
from jax.sharding import PartitionSpec as P

BLOCK = 128
STEPS = 2
ROWS_PER_STEP = 4
KMAX = 4


def transport_kernel(start_ref, off_ref, cnt_ref, col_ref, ext_ref, blk_ref, out_ref, acc_ref):
    g = pl.program_id(0)
    spec = ext_ref.shape[0]
    window = blk_ref.shape[0]
    n_ext = ext_ref.shape[1] // BLOCK
    for rr in range(ROWS_PER_STEP):
        r = g * ROWS_PER_STEP + rr
        off = off_ref[r]
        cnt = cnt_ref[r]
        base = start_ref[g]
        xs = []
        for k in range(KMAX):
            local = jnp.minimum(off + k, window - 1)
            col = jnp.clip(col_ref[base + local], 0, n_ext - 1)
            x = ext_ref[:, pl.ds(pl.multiple_of(col * BLOCK, BLOCK), BLOCK)]
            x = jnp.where(k < cnt, x, jnp.zeros_like(x))
            xs.append((local, x))
        for ic in range(BLOCK // 32):
            rows = slice(ic * 32, (ic + 1) * 32)
            accs = [None] * spec
            for local, x in xs:
                b = blk_ref[local, rows, :]
                for q in range(spec):
                    term = b * x[q:q + 1, :]
                    accs[q] = term if accs[q] is None else accs[q] + term
            for q in range(spec):
                acc_ref[q, rows, :] = accs[q]
        for q in range(spec):
            y = jnp.sum(acc_ref[q].T, axis=0, keepdims=True)
            out_ref[q:q + 1, rr * BLOCK:(rr + 1) * BLOCK] = y


def transport(ext, blocks, row_ptr, local_col):
    spec = ext.shape[0]
    slots = blocks.shape[0]
    nrows = row_ptr.shape[0] - 1
    groups = nrows // ROWS_PER_STEP
    window = ROWS_PER_STEP * KMAX
    starts = jnp.minimum(row_ptr[0:nrows:ROWS_PER_STEP], slots - window).astype(jnp.int32)
    group_of_row = jnp.arange(nrows) // ROWS_PER_STEP
    offs = (row_ptr[:-1] - starts[group_of_row]).astype(jnp.int32)
    cnts = jnp.clip(row_ptr[1:] - row_ptr[:-1], 0, KMAX).astype(jnp.int32)
    grid_spec = pltpu.PrefetchScalarGridSpec(
        num_scalar_prefetch=4,
        grid=(groups,),
        in_specs=[
            pl.BlockSpec(ext.shape, lambda g, s, o, c, l: (0, 0)),
            pl.BlockSpec((pl.Element(window), pl.Element(BLOCK), pl.Element(BLOCK)), lambda g, s, o, c, l: (s[g], 0, 0)),
        ],
        out_specs=pl.BlockSpec((spec, ROWS_PER_STEP * BLOCK), lambda g, s, o, c, l: (0, g)),
        scratch_shapes=[pltpu.VMEM((spec, BLOCK, BLOCK), jnp.float32)],
    )
    flops = 2 * slots * BLOCK * BLOCK * spec
    return pl.pallas_call(
        transport_kernel,
        grid_spec=grid_spec,
        out_shape=jax.ShapeDtypeStruct((spec, nrows * BLOCK), jnp.float32),
        cost_estimate=pl.CostEstimate(flops=flops, bytes_accessed=blocks.size * 4 + ext.size * 4, transcendentals=0),
    )(starts, offs, cnts, local_col.astype(jnp.int32), ext, blocks)


def with_halo(cells, sides, width):
    for axis, dim in sides:
        count = lax.axis_size(axis)
        head = lax.slice_in_dim(cells, 0, width, axis=dim)
        tail = lax.slice_in_dim(cells, cells.shape[dim] - width, cells.shape[dim], axis=dim)
        cells = jnp.concatenate(
            [
                lax.ppermute(tail, axis, [(i, (i + 1) % count) for i in range(count)]),
                cells,
                lax.ppermute(head, axis, [((i + 1) % count, i) for i in range(count)]),
            ],
            axis=dim,
        )
    return cells


def chemistry_local(moved, block_jac):
    spec, cells = moved.shape
    nblk = cells // BLOCK
    per_block = moved.reshape(spec, nblk, BLOCK)
    out = jnp.einsum("but,ubc->tbc", block_jac, per_block, precision=lax.Precision.HIGHEST)
    return out.reshape(spec, cells)


def body(adjoint, blocks, row_ptr, col_idx, regime, jac):
    spec_dev, cells_dev = adjoint.shape
    nb_dev = cells_dev // BLOCK
    cell_devices = lax.axis_size("cells")
    cell_index = lax.axis_index("cells")
    tracer_devices = lax.axis_size("tracer")
    tracer_index = lax.axis_index("tracer")
    nb_total = nb_dev * cell_devices
    pointers = row_ptr[0]
    slot_count = blocks.shape[0]
    slot_ids = jnp.arange(slot_count)
    live_slot = slot_ids < pointers[-1]
    local_col = jnp.mod(col_idx - (cell_index - 1) * nb_dev, nb_total)
    local_col = jnp.where(live_slot, local_col, 0)
    own_blocks = nb_dev // tracer_devices
    own_regime = lax.dynamic_slice_in_dim(regime, tracer_index * own_blocks, own_blocks)
    block_jac = jnp.take(jac, own_regime, axis=0)
    adjoint_field = adjoint
    for hour_step in range(STEPS):
        extended = with_halo(adjoint_field, (("cells", 1),), cells_dev)
        moved = transport(extended, blocks, pointers, local_col)
        split = lax.all_to_all(moved, "tracer", 1, 0, tiled=True)
        reacted = chemistry_local(split, block_jac)
        adjoint_field = lax.all_to_all(reacted, "tracer", 0, 1, tiled=True)
    return adjoint_field


def solution(mesh):
    return jax.shard_map(
        body,
        mesh=mesh,
        in_specs=(
            P("tracer", "cells"),
            P("cells", None, None),
            P("cells", None),
            P("cells"),
            P("cells"),
            P(),
        ),
        out_specs=P("tracer", "cells"),
        check_vma=False,
    )
```

```python
import jax
import jax.numpy as jnp
from jax import lax
from jax.experimental import pallas as pl
from jax.experimental.pallas import tpu as pltpu
from jax.sharding import PartitionSpec as P

BLOCK = 128
STEPS = 2
ROWS_PER_STEP = 4
KMAX = 4


def transport_kernel(rp_ref, col_ref, left_ref, mid_ref, right_ref, blk_ref, out_ref, acc_ref):
    g = pl.program_id(0)
    spec, cells = mid_ref.shape
    nb_dev = cells // BLOCK
    nb_total = nb_dev * lax.axis_size("cells")
    first = (lax.axis_index("cells") - 1) * nb_dev
    window = blk_ref.shape[0]
    slots = col_ref.shape[0]
    base = jnp.minimum(rp_ref[g * ROWS_PER_STEP], slots - window)
    for rr in range(ROWS_PER_STEP):
        r = g * ROWS_PER_STEP + rr
        start = rp_ref[r]
        cnt = rp_ref[r + 1] - start
        off = start - base
        xs = []
        for k in range(KMAX):
            local = jnp.clip(off + k, 0, window - 1)
            col = lax.rem(col_ref[base + local] - first + 2 * nb_total, nb_total)
            col = jnp.clip(col, 0, 3 * nb_dev - 1)
            piece = col // nb_dev
            lane = pl.multiple_of((col - piece * nb_dev) * BLOCK, BLOCK)
            x = jnp.where(
                piece == 0,
                left_ref[:, pl.ds(lane, BLOCK)],
                jnp.where(piece == 1, mid_ref[:, pl.ds(lane, BLOCK)], right_ref[:, pl.ds(lane, BLOCK)]),
            )
            x = jnp.where(k < cnt, x, jnp.zeros_like(x))
            xs.append((local, x))
        for ic in range(BLOCK // 32):
            rows = slice(ic * 32, (ic + 1) * 32)
            accs = [None] * spec
            for local, x in xs:
                b = blk_ref[local, rows, :]
                for q in range(spec):
                    term = b * x[q:q + 1, :]
                    accs[q] = term if accs[q] is None else accs[q] + term
            for q in range(spec):
                acc_ref[q, rows, :] = accs[q]
        for q in range(spec):
            y = jnp.sum(acc_ref[q].T, axis=0, keepdims=True)
            out_ref[q:q + 1, rr * BLOCK:(rr + 1) * BLOCK] = y


def transport(left, mid, right, blocks, row_ptr, col_idx):
    spec, cells = mid.shape
    slots = blocks.shape[0]
    nrows = row_ptr.shape[0] - 1
    groups = nrows // ROWS_PER_STEP
    window = ROWS_PER_STEP * KMAX
    whole = lambda g, rp, ci: (0, 0)
    grid_spec = pltpu.PrefetchScalarGridSpec(
        num_scalar_prefetch=2,
        grid=(groups,),
        in_specs=[
            pl.BlockSpec(mid.shape, whole),
            pl.BlockSpec(mid.shape, whole),
            pl.BlockSpec(mid.shape, whole),
            pl.BlockSpec(
                (pl.Element(window), pl.Element(BLOCK), pl.Element(BLOCK)),
                lambda g, rp, ci: (jnp.minimum(rp[g * ROWS_PER_STEP], slots - window), 0, 0),
            ),
        ],
        out_specs=pl.BlockSpec((spec, ROWS_PER_STEP * BLOCK), lambda g, rp, ci: (0, g)),
        scratch_shapes=[pltpu.VMEM((spec, BLOCK, BLOCK), jnp.float32)],
    )
    flops = 2 * slots * BLOCK * BLOCK * spec
    return pl.pallas_call(
        transport_kernel,
        grid_spec=grid_spec,
        out_shape=jax.ShapeDtypeStruct((spec, nrows * BLOCK), jnp.float32),
        cost_estimate=pl.CostEstimate(
            flops=flops, bytes_accessed=blocks.size * 4 + 4 * mid.size * 4, transcendentals=0
        ),
    )(row_ptr, col_idx, left, mid, right, blocks)


def chemistry_local(moved, block_jac):
    spec, cells = moved.shape
    nblk = cells // BLOCK
    per_block = moved.reshape(spec, nblk, BLOCK)
    out = jnp.einsum("but,ubc->tbc", block_jac, per_block, precision=lax.Precision.HIGHEST)
    return out.reshape(spec, cells)


def halo(field):
    count = lax.axis_size("cells")
    left = lax.ppermute(field, "cells", [(i, (i + 1) % count) for i in range(count)])
    right = lax.ppermute(field, "cells", [((i + 1) % count, i) for i in range(count)])
    return left, right


def body(adjoint, blocks, row_ptr, col_idx, regime, jac):
    spec_dev, cells_dev = adjoint.shape
    nb_dev = cells_dev // BLOCK
    tracer_devices = lax.axis_size("tracer")
    tracer_index = lax.axis_index("tracer")
    pointers = row_ptr.reshape(-1)
    own_blocks = nb_dev // tracer_devices
    own_regime = lax.dynamic_slice_in_dim(regime, tracer_index * own_blocks, own_blocks)
    block_jac = jnp.take(jac, own_regime, axis=0)
    adjoint_field = adjoint
    for hour_step in range(STEPS):
        left, right = halo(adjoint_field)
        moved = transport(left, adjoint_field, right, blocks, pointers, col_idx)
        split = lax.all_to_all(moved, "tracer", 1, 0, tiled=True)
        reacted = chemistry_local(split, block_jac)
        adjoint_field = lax.all_to_all(reacted, "tracer", 0, 1, tiled=True)
    return adjoint_field


def solution(mesh):
    return jax.shard_map(
        body,
        mesh=mesh,
        in_specs=(
            P("tracer", "cells"),
            P("cells", None, None),
            P("cells", None),
            P("cells"),
            P("cells"),
            P(),
        ),
        out_specs=P("tracer", "cells"),
        check_vma=False,
    )
```

```python
import jax
import jax.numpy as jnp
from jax import lax
from jax.experimental import pallas as pl
from jax.experimental.pallas import tpu as pltpu
from jax.sharding import PartitionSpec as P

BLOCK = 128
STEPS = 2
ROWS_PER_STEP = 4
KMAX = 4


def transport_kernel(rp_ref, col_ref, left_ref, mid_ref, right_ref, blk_ref, out_ref, acc_ref):
    g = pl.program_id(0)
    spec, cells = mid_ref.shape
    nb_dev = cells // BLOCK
    nb_total = nb_dev * lax.axis_size("cells")
    first = (lax.axis_index("cells") - 1) * nb_dev
    window = blk_ref.shape[0]
    slots = col_ref.shape[0]
    base = jnp.minimum(rp_ref[g * ROWS_PER_STEP], slots - window)
    for rr in range(ROWS_PER_STEP):
        r = g * ROWS_PER_STEP + rr
        start = rp_ref[r]
        cnt = rp_ref[r + 1] - start
        off = start - base
        xs = []
        for k in range(KMAX):
            local = jnp.clip(off + k, 0, window - 1)
            col = lax.rem(col_ref[base + local] - first + 2 * nb_total, nb_total)
            col = jnp.clip(col, 0, 3 * nb_dev - 1)
            piece = col // nb_dev
            lane = pl.multiple_of((col - piece * nb_dev) * BLOCK, BLOCK)
            x = jnp.where(
                piece == 0,
                left_ref[:, pl.ds(lane, BLOCK)],
                jnp.where(piece == 1, mid_ref[:, pl.ds(lane, BLOCK)], right_ref[:, pl.ds(lane, BLOCK)]),
            )
            x = jnp.where(k < cnt, x, jnp.zeros_like(x))
            xs.append((local, x))
        for ic in range(BLOCK // 32):
            rows = slice(ic * 32, (ic + 1) * 32)
            accs = [None] * spec
            for local, x in xs:
                b = blk_ref[local, rows, :]
                for q in range(spec):
                    term = b * x[q:q + 1, :]
                    accs[q] = term if accs[q] is None else accs[q] + term
            for q in range(spec):
                acc_ref[q, rows, :] = accs[q]
        for q in range(spec):
            y = jnp.sum(acc_ref[q].T, axis=0, keepdims=True)
            out_ref[q:q + 1, rr * BLOCK:(rr + 1) * BLOCK] = y


def transport(left, mid, right, blocks, row_ptr, col_idx):
    spec, cells = mid.shape
    slots = blocks.shape[0]
    nrows = row_ptr.shape[0] - 1
    groups = nrows // ROWS_PER_STEP
    window = ROWS_PER_STEP * KMAX
    whole = lambda g, rp, ci: (0, 0)
    grid_spec = pltpu.PrefetchScalarGridSpec(
        num_scalar_prefetch=2,
        grid=(groups,),
        in_specs=[
            pl.BlockSpec(mid.shape, whole),
            pl.BlockSpec(mid.shape, whole),
            pl.BlockSpec(mid.shape, whole),
            pl.BlockSpec(
                (pl.Element(window), pl.Element(BLOCK), pl.Element(BLOCK)),
                lambda g, rp, ci: (jnp.minimum(rp[g * ROWS_PER_STEP], slots - window), 0, 0),
            ),
        ],
        out_specs=pl.BlockSpec((spec, ROWS_PER_STEP * BLOCK), lambda g, rp, ci: (0, g)),
        scratch_shapes=[pltpu.VMEM((spec, BLOCK, BLOCK), jnp.float32)],
    )
    flops = 2 * slots * BLOCK * BLOCK * spec
    return pl.pallas_call(
        transport_kernel,
        grid_spec=grid_spec,
        out_shape=jax.ShapeDtypeStruct((spec, nrows * BLOCK), jnp.float32),
        cost_estimate=pl.CostEstimate(
            flops=flops, bytes_accessed=blocks.size * 4 + 4 * mid.size * 4, transcendentals=0
        ),
    )(row_ptr, col_idx, left, mid, right, blocks)


def chemistry_own(moved_all, block_jac):
    spec, cells = moved_all.shape
    nblk = cells // BLOCK
    per_block = moved_all.reshape(spec, nblk, BLOCK)
    out = jnp.einsum("but,ubc->tbc", block_jac, per_block, precision=lax.Precision.HIGHEST)
    return out.reshape(out.shape[0], cells)


def gather_species(moved):
    peers = lax.axis_size("tracer")
    copies = jnp.broadcast_to(moved[None], (peers,) + moved.shape)
    every = lax.all_to_all(copies, "tracer", 0, 0, tiled=True)
    return every.reshape(peers * moved.shape[0], moved.shape[1])


def halo(field):
    count = lax.axis_size("cells")
    left = lax.ppermute(field, "cells", [(i, (i + 1) % count) for i in range(count)])
    right = lax.ppermute(field, "cells", [((i + 1) % count, i) for i in range(count)])
    return left, right


def body(adjoint, blocks, row_ptr, col_idx, regime, jac):
    spec_dev, cells_dev = adjoint.shape
    nb_dev = cells_dev // BLOCK
    tracer_index = lax.axis_index("tracer")
    pointers = row_ptr.reshape(-1)
    own_jac = lax.dynamic_slice_in_dim(jac, tracer_index * spec_dev, spec_dev, 2)
    block_jac = jnp.take(own_jac, regime, axis=0)
    adjoint_field = adjoint
    for hour_step in range(STEPS):
        left, right = halo(adjoint_field)
        moved = transport(left, adjoint_field, right, blocks, pointers, col_idx)
        adjoint_field = chemistry_own(gather_species(moved), block_jac)
    return adjoint_field


def solution(mesh):
    return jax.shard_map(
        body,
        mesh=mesh,
        in_specs=(
            P("tracer", "cells"),
            P("cells", None, None),
            P("cells", None),
            P("cells"),
            P("cells"),
            P(),
        ),
        out_specs=P("tracer", "cells"),
        check_vma=False,
    )
```

```python
import jax
import jax.numpy as jnp
from jax import lax
from jax.experimental import pallas as pl
from jax.experimental.pallas import tpu as pltpu
from jax.sharding import PartitionSpec as P

BLOCK = 128
STEPS = 2
ROWS_PER_STEP = 4
KMAX = 4


def transport_kernel(rp_ref, col_ref, left_ref, mid_ref, right_ref, blk_ref, out_ref, acc_ref):
    g = pl.program_id(0)
    spec, cells = mid_ref.shape
    nb_dev = cells // BLOCK
    nb_total = nb_dev * lax.axis_size("cells")
    first = (lax.axis_index("cells") - 1) * nb_dev
    window = blk_ref.shape[0]
    slots = col_ref.shape[0]
    base = jnp.minimum(rp_ref[g * ROWS_PER_STEP], slots - window)
    for rr in range(ROWS_PER_STEP):
        r = g * ROWS_PER_STEP + rr
        start = rp_ref[r]
        cnt = rp_ref[r + 1] - start
        off = start - base
        xs = []
        for k in range(KMAX):
            local = jnp.clip(off + k, 0, window - 1)
            col = lax.rem(col_ref[base + local] - first + 2 * nb_total, nb_total)
            col = jnp.clip(col, 0, 3 * nb_dev - 1)
            piece = col // nb_dev
            lane = pl.multiple_of((col - piece * nb_dev) * BLOCK, BLOCK)
            x = jnp.where(
                piece == 0,
                left_ref[:, pl.ds(lane, BLOCK)],
                jnp.where(piece == 1, mid_ref[:, pl.ds(lane, BLOCK)], right_ref[:, pl.ds(lane, BLOCK)]),
            )
            x = jnp.where(k < cnt, x, jnp.zeros_like(x))
            xs.append((local, x))
        for ic in range(BLOCK // 32):
            rows = slice(ic * 32, (ic + 1) * 32)
            accs = [None] * spec
            for local, x in xs:
                b = blk_ref[local, rows, :]
                for q in range(spec):
                    term = b * x[q:q + 1, :]
                    accs[q] = term if accs[q] is None else accs[q] + term
            for q in range(spec):
                acc_ref[q, rows, :] = accs[q]
        for q in range(spec):
            y = jnp.sum(acc_ref[q].T, axis=0, keepdims=True)
            out_ref[q:q + 1, rr * BLOCK:(rr + 1) * BLOCK] = y


def transport(left, mid, right, blocks, row_ptr, col_idx):
    spec, cells = mid.shape
    slots = blocks.shape[0]
    nrows = row_ptr.shape[0] - 1
    groups = nrows // ROWS_PER_STEP
    window = ROWS_PER_STEP * KMAX
    whole = lambda g, rp, ci: (0, 0)
    grid_spec = pltpu.PrefetchScalarGridSpec(
        num_scalar_prefetch=2,
        grid=(groups,),
        in_specs=[
            pl.BlockSpec(mid.shape, whole),
            pl.BlockSpec(mid.shape, whole),
            pl.BlockSpec(mid.shape, whole),
            pl.BlockSpec(
                (pl.Element(window), pl.Element(BLOCK), pl.Element(BLOCK)),
                lambda g, rp, ci: (jnp.minimum(rp[g * ROWS_PER_STEP], slots - window), 0, 0),
            ),
        ],
        out_specs=pl.BlockSpec((spec, ROWS_PER_STEP * BLOCK), lambda g, rp, ci: (0, g)),
        scratch_shapes=[pltpu.VMEM((spec, BLOCK, BLOCK), jnp.float32)],
    )
    flops = 2 * slots * BLOCK * BLOCK * spec
    return pl.pallas_call(
        transport_kernel,
        grid_spec=grid_spec,
        out_shape=jax.ShapeDtypeStruct((spec, nrows * BLOCK), jnp.float32),
        cost_estimate=pl.CostEstimate(
            flops=flops, bytes_accessed=blocks.size * 4 + 4 * mid.size * 4, transcendentals=0
        ),
    )(row_ptr, col_idx, left, mid, right, blocks)


def chemistry_local(moved, block_jac):
    spec, cells = moved.shape
    nblk = cells // BLOCK
    per_block = moved.reshape(spec, nblk, BLOCK)
    out = jnp.einsum("but,ubc->tbc", block_jac, per_block, precision=lax.Precision.HIGHEST)
    return out.reshape(spec, cells)


def halo(field):
    count = lax.axis_size("cells")
    left = lax.ppermute(field, "cells", [(i, (i + 1) % count) for i in range(count)])
    right = lax.ppermute(field, "cells", [((i + 1) % count, i) for i in range(count)])
    return left, right


def body(adjoint, blocks, row_ptr, col_idx, regime, jac):
    spec_dev, cells_dev = adjoint.shape
    nb_dev = cells_dev // BLOCK
    tracer_devices = lax.axis_size("tracer")
    tracer_index = lax.axis_index("tracer")
    pointers = row_ptr.reshape(-1)
    own_blocks = nb_dev // tracer_devices
    own_regime = lax.dynamic_slice_in_dim(regime, tracer_index * own_blocks, own_blocks)
    block_jac = jnp.take(jac, own_regime, axis=0)
    adjoint_field = adjoint
    for hour_step in range(STEPS):
        left, right = halo(adjoint_field)
        moved = transport(left, adjoint_field, right, blocks, pointers, col_idx)
        if hour_step == 0:
            moved, block_jac = lax.optimization_barrier((moved, block_jac))
        split = lax.all_to_all(moved, "tracer", 1, 0, tiled=True)
        reacted = chemistry_local(split, block_jac)
        adjoint_field = lax.all_to_all(reacted, "tracer", 0, 1, tiled=True)
    return adjoint_field


def solution(mesh):
    return jax.shard_map(
        body,
        mesh=mesh,
        in_specs=(
            P("tracer", "cells"),
            P("cells", None, None),
            P("cells", None),
            P("cells"),
            P("cells"),
            P(),
        ),
        out_specs=P("tracer", "cells"),
        check_vma=False,
    )
```

```python
import jax
import jax.numpy as jnp
from jax import lax
from jax.experimental import pallas as pl
from jax.experimental.pallas import tpu as pltpu
from jax.sharding import PartitionSpec as P

BLOCK = 128
STEPS = 2
ROWS_PER_STEP = 4
KMAX = 4


def transport_kernel(rp_ref, col_ref, left_ref, mid_ref, right_ref, blk_ref, out_ref, acc_ref):
    g = pl.program_id(0)
    spec, cells = mid_ref.shape
    nb_dev = cells // BLOCK
    nb_total = nb_dev * lax.axis_size("cells")
    first = (lax.axis_index("cells") - 1) * nb_dev
    window = blk_ref.shape[0]
    slots = col_ref.shape[0]
    base = jnp.minimum(rp_ref[g * ROWS_PER_STEP], slots - window)
    for rr in range(ROWS_PER_STEP):
        r = g * ROWS_PER_STEP + rr
        start = rp_ref[r]
        cnt = rp_ref[r + 1] - start
        off = start - base
        xs = []
        for k in range(KMAX):
            local = jnp.clip(off + k, 0, window - 1)
            col = lax.rem(col_ref[base + local] - first + 2 * nb_total, nb_total)
            col = jnp.clip(col, 0, 3 * nb_dev - 1)
            piece = col // nb_dev
            lane = pl.multiple_of((col - piece * nb_dev) * BLOCK, BLOCK)
            x = jnp.where(
                piece == 0,
                left_ref[:, pl.ds(lane, BLOCK)],
                jnp.where(piece == 1, mid_ref[:, pl.ds(lane, BLOCK)], right_ref[:, pl.ds(lane, BLOCK)]),
            )
            x = jnp.where(k < cnt, x, jnp.zeros_like(x))
            xs.append((local, x))
        for ic in range(BLOCK // 32):
            rows = slice(ic * 32, (ic + 1) * 32)
            accs = [None] * spec
            for local, x in xs:
                b = blk_ref[local, rows, :]
                for q in range(spec):
                    term = b * x[q:q + 1, :]
                    accs[q] = term if accs[q] is None else accs[q] + term
            for q in range(spec):
                acc_ref[q, rows, :] = accs[q]
        for q in range(spec):
            y = jnp.sum(acc_ref[q].T, axis=0, keepdims=True)
            out_ref[q:q + 1, rr * BLOCK:(rr + 1) * BLOCK] = y


def transport(left, mid, right, blocks, row_ptr, col_idx):
    spec, cells = mid.shape
    slots = blocks.shape[0]
    nrows = row_ptr.shape[0] - 1
    groups = nrows // ROWS_PER_STEP
    window = ROWS_PER_STEP * KMAX
    whole = lambda g, rp, ci: (0, 0)
    grid_spec = pltpu.PrefetchScalarGridSpec(
        num_scalar_prefetch=2,
        grid=(groups,),
        in_specs=[
            pl.BlockSpec(mid.shape, whole),
            pl.BlockSpec(mid.shape, whole),
            pl.BlockSpec(mid.shape, whole),
            pl.BlockSpec(
                (pl.Element(window), pl.Element(BLOCK), pl.Element(BLOCK)),
                lambda g, rp, ci: (jnp.minimum(rp[g * ROWS_PER_STEP], slots - window), 0, 0),
            ),
        ],
        out_specs=pl.BlockSpec((spec, ROWS_PER_STEP * BLOCK), lambda g, rp, ci: (0, g)),
        scratch_shapes=[pltpu.VMEM((spec, BLOCK, BLOCK), jnp.float32)],
    )
    flops = 2 * slots * BLOCK * BLOCK * spec
    return pl.pallas_call(
        transport_kernel,
        grid_spec=grid_spec,
        out_shape=jax.ShapeDtypeStruct((spec, nrows * BLOCK), jnp.float32),
        cost_estimate=pl.CostEstimate(
            flops=flops, bytes_accessed=blocks.size * 4 + 4 * mid.size * 4, transcendentals=0
        ),
    )(row_ptr, col_idx, left, mid, right, blocks)


def chemistry_local(moved, block_jac):
    spec, cells = moved.shape
    nblk = cells // BLOCK
    per_block = moved.reshape(spec, nblk, BLOCK)
    out = jnp.einsum("but,ubc->tbc", block_jac, per_block, precision=lax.Precision.HIGHEST)
    return out.reshape(spec, cells)


def slot_kernel(rp_ref, col_ref, left_ref, mid_ref, right_ref, blk_ref, out_ref):
    g = pl.program_id(0)
    spec, cells = mid_ref.shape
    nb_dev = cells // BLOCK
    nb_total = nb_dev * lax.axis_size("cells")
    first = (lax.axis_index("cells") - 1) * nb_dev
    window = blk_ref.shape[0]
    slots = col_ref.shape[0]
    base = jnp.minimum(rp_ref[g * ROWS_PER_STEP], slots - window)
    for rr in range(ROWS_PER_STEP):
        r = g * ROWS_PER_STEP + rr
        start = rp_ref[r]
        cnt = rp_ref[r + 1] - start
        off = start - base
        for k in range(KMAX):
            local = jnp.clip(off + k, 0, window - 1)
            col = lax.rem(col_ref[base + local] - first + 2 * nb_total, nb_total)
            col = jnp.clip(col, 0, 3 * nb_dev - 1)
            piece = col // nb_dev
            lane = pl.multiple_of((col - piece * nb_dev) * BLOCK, BLOCK)
            x = jnp.where(
                piece == 0,
                left_ref[:, pl.ds(lane, BLOCK)],
                jnp.where(piece == 1, mid_ref[:, pl.ds(lane, BLOCK)], right_ref[:, pl.ds(lane, BLOCK)]),
            )
            x = jnp.where(k < cnt, x, jnp.zeros_like(x))
            out_ref[rr, k] = lax.dot_general(
                x, blk_ref[local], (((1,), (1,)), ((), ())),
                precision=lax.Precision.HIGHEST, preferred_element_type=jnp.float32,
            )


def transport_slots(left, mid, right, blocks, row_ptr, col_idx):
    spec, cells = mid.shape
    slots = blocks.shape[0]
    nrows = row_ptr.shape[0] - 1
    groups = nrows // ROWS_PER_STEP
    window = ROWS_PER_STEP * KMAX
    whole = lambda g, rp, ci: (0, 0)
    grid_spec = pltpu.PrefetchScalarGridSpec(
        num_scalar_prefetch=2,
        grid=(groups,),
        in_specs=[
            pl.BlockSpec(mid.shape, whole),
            pl.BlockSpec(mid.shape, whole),
            pl.BlockSpec(mid.shape, whole),
            pl.BlockSpec(
                (pl.Element(window), pl.Element(BLOCK), pl.Element(BLOCK)),
                lambda g, rp, ci: (jnp.minimum(rp[g * ROWS_PER_STEP], slots - window), 0, 0),
            ),
        ],
        out_specs=pl.BlockSpec((ROWS_PER_STEP, KMAX, spec, BLOCK), lambda g, rp, ci: (g, 0, 0, 0)),
    )
    return pl.pallas_call(
        slot_kernel,
        grid_spec=grid_spec,
        out_shape=jax.ShapeDtypeStruct((nrows, KMAX, spec, BLOCK), jnp.float32),
        cost_estimate=pl.CostEstimate(
            flops=2 * slots * BLOCK * BLOCK * spec, bytes_accessed=blocks.size * 4, transcendentals=0
        ),
    )(row_ptr, col_idx, left, mid, right, blocks)


def halo(field):
    count = lax.axis_size("cells")
    left = lax.ppermute(field, "cells", [(i, (i + 1) % count) for i in range(count)])
    right = lax.ppermute(field, "cells", [((i + 1) % count, i) for i in range(count)])
    return left, right


def body(adjoint, blocks, row_ptr, col_idx, regime, jac):
    spec_dev, cells_dev = adjoint.shape
    nb_dev = cells_dev // BLOCK
    nb_total = nb_dev * lax.axis_size("cells")
    cell_index = lax.axis_index("cells")
    tracer_devices = lax.axis_size("tracer")
    tracer_index = lax.axis_index("tracer")
    pointers = row_ptr.reshape(-1)
    own_rows = nb_dev // tracer_devices
    left, right = halo(adjoint)
    moved = transport(left, adjoint, right, blocks, pointers, col_idx)
    left, right = halo(moved)
    per_slot = transport_slots(left, moved, right, blocks, pointers, col_idx)
    split = lax.all_to_all(per_slot, "tracer", 0, 2, tiled=True)
    reg_left, reg_right = halo(regime)
    regime_ext = jnp.concatenate([reg_left, regime, reg_right])
    rows = tracer_index * own_rows + jnp.arange(own_rows)
    slot = jnp.minimum(pointers[rows][:, None] + jnp.arange(KMAX)[None, :], col_idx.shape[0] - 1)
    local_col = jnp.mod(col_idx[slot] - (cell_index - 1) * nb_dev, nb_total)
    local_col = jnp.clip(local_col, 0, 3 * nb_dev - 1)
    jac_col = jnp.take(jac, regime_ext[local_col], axis=0)
    jac_row = jnp.take(jac, regime[rows], axis=0)
    combined = jnp.einsum("gkvu,gut->gkvt", jac_col, jac_row, precision=lax.Precision.HIGHEST)
    reacted = jnp.einsum("gkvt,gkvc->tgc", combined, split, precision=lax.Precision.HIGHEST)
    reacted = reacted.reshape(reacted.shape[0], own_rows * BLOCK)
    return lax.all_to_all(reacted, "tracer", 0, 1, tiled=True)


def solution(mesh):
    return jax.shard_map(
        body,
        mesh=mesh,
        in_specs=(
            P("tracer", "cells"),
            P("cells", None, None),
            P("cells", None),
            P("cells"),
            P("cells"),
            P(),
        ),
        out_specs=P("tracer", "cells"),
        check_vma=False,
    )
```

```python
import jax
import jax.numpy as jnp
from jax import lax
from jax.experimental import pallas as pl
from jax.experimental.pallas import tpu as pltpu
from jax.sharding import PartitionSpec as P

BLOCK = 128
STEPS = 2
ROWS_PER_STEP = 4
KMAX = 4


def transport_kernel(rp_ref, col_ref, left_ref, mid_ref, right_ref, blk_ref, out_ref, acc_ref):
    g = pl.program_id(0)
    spec, cells = mid_ref.shape
    nb_dev = cells // BLOCK
    nb_total = nb_dev * lax.axis_size("cells")
    first = (lax.axis_index("cells") - 1) * nb_dev
    window = blk_ref.shape[0]
    slots = col_ref.shape[0]
    base = jnp.minimum(rp_ref[g * ROWS_PER_STEP], slots - window)
    for rr in range(ROWS_PER_STEP):
        r = g * ROWS_PER_STEP + rr
        start = rp_ref[r]
        cnt = rp_ref[r + 1] - start
        off = start - base
        xs = []
        for k in range(KMAX):
            local = jnp.clip(off + k, 0, window - 1)
            col = lax.rem(col_ref[base + local] - first + 2 * nb_total, nb_total)
            col = jnp.clip(col, 0, 3 * nb_dev - 1)
            piece = col // nb_dev
            lane = pl.multiple_of((col - piece * nb_dev) * BLOCK, BLOCK)
            x = jnp.where(
                piece == 0,
                left_ref[0:spec, pl.ds(lane, BLOCK)],
                jnp.where(piece == 1, mid_ref[:, pl.ds(lane, BLOCK)], right_ref[0:spec, pl.ds(lane, BLOCK)]),
            )
            x = jnp.where(k < cnt, x, jnp.zeros_like(x))
            xs.append((local, x))
        for ic in range(BLOCK // 32):
            rows = slice(ic * 32, (ic + 1) * 32)
            accs = [None] * spec
            for local, x in xs:
                b = blk_ref[local, rows, :]
                for q in range(spec):
                    term = b * x[q:q + 1, :]
                    accs[q] = term if accs[q] is None else accs[q] + term
            for q in range(spec):
                acc_ref[q, rows, :] = accs[q]
        for q in range(spec):
            y = jnp.sum(acc_ref[q].T, axis=0, keepdims=True)
            out_ref[q:q + 1, rr * BLOCK:(rr + 1) * BLOCK] = y


def transport(left, mid, right, blocks, row_ptr, col_idx):
    spec, cells = mid.shape
    slots = blocks.shape[0]
    nrows = row_ptr.shape[0] - 1
    groups = nrows // ROWS_PER_STEP
    window = ROWS_PER_STEP * KMAX
    whole = lambda g, rp, ci: (0, 0)
    grid_spec = pltpu.PrefetchScalarGridSpec(
        num_scalar_prefetch=2,
        grid=(groups,),
        in_specs=[
            pl.BlockSpec(left.shape, whole),
            pl.BlockSpec(mid.shape, whole),
            pl.BlockSpec(right.shape, whole),
            pl.BlockSpec(
                (pl.Element(window), pl.Element(BLOCK), pl.Element(BLOCK)),
                lambda g, rp, ci: (jnp.minimum(rp[g * ROWS_PER_STEP], slots - window), 0, 0),
            ),
        ],
        out_specs=pl.BlockSpec((spec, ROWS_PER_STEP * BLOCK), lambda g, rp, ci: (0, g)),
        scratch_shapes=[pltpu.VMEM((spec, BLOCK, BLOCK), jnp.float32)],
    )
    flops = 2 * slots * BLOCK * BLOCK * spec
    return pl.pallas_call(
        transport_kernel,
        grid_spec=grid_spec,
        out_shape=jax.ShapeDtypeStruct((spec, nrows * BLOCK), jnp.float32),
        cost_estimate=pl.CostEstimate(
            flops=flops, bytes_accessed=blocks.size * 4 + 4 * mid.size * 4, transcendentals=0
        ),
    )(row_ptr, col_idx, left, mid, right, blocks)


def chemistry_local(moved, block_jac):
    spec, cells = moved.shape
    nblk = cells // BLOCK
    per_block = moved.reshape(spec, nblk, BLOCK)
    out = jnp.einsum("but,ubc->tbc", block_jac, per_block, precision=lax.Precision.HIGHEST)
    return out.reshape(spec, cells)


def slot_kernel(rp_ref, col_ref, left_ref, mid_ref, right_ref, blk_ref, out_ref):
    g = pl.program_id(0)
    spec, cells = mid_ref.shape
    nb_dev = cells // BLOCK
    nb_total = nb_dev * lax.axis_size("cells")
    first = (lax.axis_index("cells") - 1) * nb_dev
    window = blk_ref.shape[0]
    slots = col_ref.shape[0]
    base = jnp.minimum(rp_ref[g * ROWS_PER_STEP], slots - window)
    for rr in range(ROWS_PER_STEP):
        r = g * ROWS_PER_STEP + rr
        start = rp_ref[r]
        cnt = rp_ref[r + 1] - start
        off = start - base
        for k in range(KMAX):
            local = jnp.clip(off + k, 0, window - 1)
            col = lax.rem(col_ref[base + local] - first + 2 * nb_total, nb_total)
            col = jnp.clip(col, 0, 3 * nb_dev - 1)
            piece = col // nb_dev
            lane = pl.multiple_of((col - piece * nb_dev) * BLOCK, BLOCK)
            x = jnp.where(
                piece == 0,
                left_ref[:, pl.ds(lane, BLOCK)],
                jnp.where(piece == 1, mid_ref[:, pl.ds(lane, BLOCK)], right_ref[:, pl.ds(lane, BLOCK)]),
            )
            x = jnp.where(k < cnt, x, jnp.zeros_like(x))
            out_ref[rr, k] = lax.dot_general(
                x, blk_ref[local], (((1,), (1,)), ((), ())),
                precision=lax.Precision.HIGHEST, preferred_element_type=jnp.float32,
            )


def transport_slots(left, mid, right, blocks, row_ptr, col_idx):
    spec, cells = mid.shape
    slots = blocks.shape[0]
    nrows = row_ptr.shape[0] - 1
    groups = nrows // ROWS_PER_STEP
    window = ROWS_PER_STEP * KMAX
    whole = lambda g, rp, ci: (0, 0)
    grid_spec = pltpu.PrefetchScalarGridSpec(
        num_scalar_prefetch=2,
        grid=(groups,),
        in_specs=[
            pl.BlockSpec(mid.shape, whole),
            pl.BlockSpec(mid.shape, whole),
            pl.BlockSpec(mid.shape, whole),
            pl.BlockSpec(
                (pl.Element(window), pl.Element(BLOCK), pl.Element(BLOCK)),
                lambda g, rp, ci: (jnp.minimum(rp[g * ROWS_PER_STEP], slots - window), 0, 0),
            ),
        ],
        out_specs=pl.BlockSpec((ROWS_PER_STEP, KMAX, spec, BLOCK), lambda g, rp, ci: (g, 0, 0, 0)),
    )
    return pl.pallas_call(
        slot_kernel,
        grid_spec=grid_spec,
        out_shape=jax.ShapeDtypeStruct((nrows, KMAX, spec, BLOCK), jnp.float32),
        cost_estimate=pl.CostEstimate(
            flops=2 * slots * BLOCK * BLOCK * spec, bytes_accessed=blocks.size * 4, transcendentals=0
        ),
    )(row_ptr, col_idx, left, mid, right, blocks)


def combine_kernel(rp_ref, col_ref, reg_ref, jac_ref, out_ref):
    own_rows = out_ref.shape[0]
    slots = col_ref.shape[0]
    nb_dev = reg_ref.shape[0] // 3
    nb_total = nb_dev * lax.axis_size("cells")
    first = (lax.axis_index("cells") - 1) * nb_dev
    for g in range(own_rows):
        row = lax.axis_index("tracer") * own_rows + g
        nreg = jac_ref.shape[0]
        row_jac = jac_ref[jnp.clip(reg_ref[nb_dev + row], 0, nreg - 1)]
        for k in range(KMAX):
            slot = jnp.minimum(rp_ref[row] + k, slots - 1)
            col = lax.rem(col_ref[slot] - first + 2 * nb_total, nb_total)
            col = jnp.clip(col, 0, 3 * nb_dev - 1)
            out_ref[g, k] = jnp.dot(
                jac_ref[jnp.clip(reg_ref[col], 0, nreg - 1)], row_jac,
                precision=lax.Precision.HIGHEST, preferred_element_type=jnp.float32,
            )


def combined_jac(row_ptr, col_idx, regime_ext, jac, own_rows):
    nreg, spec, _ = jac.shape
    grid_spec = pltpu.PrefetchScalarGridSpec(
        num_scalar_prefetch=3,
        grid=(1,),
        in_specs=[pl.BlockSpec(jac.shape, lambda i, rp, ci, rg: (0, 0, 0))],
        out_specs=pl.BlockSpec((own_rows, KMAX, spec, spec), lambda i, rp, ci, rg: (0, 0, 0, 0)),
    )
    return pl.pallas_call(
        combine_kernel,
        grid_spec=grid_spec,
        out_shape=jax.ShapeDtypeStruct((own_rows, KMAX, spec, spec), jnp.float32),
    )(row_ptr, col_idx, regime_ext, jac)


def halo(field):
    count = lax.axis_size("cells")
    left = lax.ppermute(field, "cells", [(i, (i + 1) % count) for i in range(count)])
    right = lax.ppermute(field, "cells", [((i + 1) % count, i) for i in range(count)])
    return left, right


def body(adjoint, blocks, row_ptr, col_idx, regime, jac):
    spec_dev, cells_dev = adjoint.shape
    nb_dev = cells_dev // BLOCK
    nb_total = nb_dev * lax.axis_size("cells")
    cell_index = lax.axis_index("cells")
    tracer_devices = lax.axis_size("tracer")
    tracer_index = lax.axis_index("tracer")
    pointers = row_ptr.reshape(-1)
    own_rows = nb_dev // tracer_devices
    regime_row = jnp.zeros((1, cells_dev), jnp.float32).at[0, :nb_dev].set(regime.astype(jnp.float32))
    left, right = halo(jnp.concatenate([adjoint, regime_row], axis=0))
    moved = transport(left, adjoint, right, blocks, pointers, col_idx)
    regime_ext = jnp.concatenate(
        [left[spec_dev, :nb_dev], regime_row[0, :nb_dev], right[spec_dev, :nb_dev]]
    ).astype(jnp.int32)
    left, right = halo(moved)
    per_slot = transport_slots(left, moved, right, blocks, pointers, col_idx)
    split = lax.all_to_all(per_slot, "tracer", 0, 2, tiled=True)
    combined = combined_jac(pointers, col_idx, regime_ext, jac, own_rows)
    reacted = jnp.einsum("gkvt,gkvc->tgc", combined, split, precision=lax.Precision.HIGHEST)
    reacted = reacted.reshape(reacted.shape[0], own_rows * BLOCK)
    return lax.all_to_all(reacted, "tracer", 0, 1, tiled=True)


def solution(mesh):
    return jax.shard_map(
        body,
        mesh=mesh,
        in_specs=(
            P("tracer", "cells"),
            P("cells", None, None),
            P("cells", None),
            P("cells"),
            P("cells"),
            P(),
        ),
        out_specs=P("tracer", "cells"),
        check_vma=False,
    )
```

```python
import jax
import jax.numpy as jnp
from jax import lax
from jax.experimental import pallas as pl
from jax.experimental.pallas import tpu as pltpu
from jax.sharding import PartitionSpec as P

BLOCK = 128
STEPS = 2
ROWS_PER_STEP = 4
KMAX = 4


def transport_kernel(rp_ref, col_ref, reg_ref, left_ref, mid_ref, right_ref, blk_ref, out_ref, acc_ref):
    g = pl.program_id(0)
    spec, cells = mid_ref.shape
    nb_dev = cells // BLOCK
    nb_total = nb_dev * lax.axis_size("cells")
    first = (lax.axis_index("cells") - 1) * nb_dev
    window = blk_ref.shape[0]
    slots = col_ref.shape[0]
    base = jnp.minimum(rp_ref[g * ROWS_PER_STEP], slots - window)
    for rr in range(ROWS_PER_STEP):
        r = g * ROWS_PER_STEP + rr
        start = rp_ref[r]
        cnt = rp_ref[r + 1] - start
        off = start - base
        xs = []
        for k in range(KMAX):
            local = jnp.clip(off + k, 0, window - 1)
            col = lax.rem(col_ref[base + local] - first + 2 * nb_total, nb_total)
            col = jnp.clip(col, 0, 3 * nb_dev - 1)
            piece = col // nb_dev
            lane = pl.multiple_of((col - piece * nb_dev) * BLOCK, BLOCK)
            x = jnp.where(
                piece == 0,
                left_ref[0:spec, pl.ds(lane, BLOCK)],
                jnp.where(piece == 1, mid_ref[:, pl.ds(lane, BLOCK)], right_ref[0:spec, pl.ds(lane, BLOCK)]),
            )
            x = jnp.where(k < cnt, x, jnp.zeros_like(x))
            xs.append((local, x))
        for ic in range(BLOCK // 32):
            rows = slice(ic * 32, (ic + 1) * 32)
            accs = [None] * spec
            for local, x in xs:
                b = blk_ref[local, rows, :]
                for q in range(spec):
                    term = b * x[q:q + 1, :]
                    accs[q] = term if accs[q] is None else accs[q] + term
            for q in range(spec):
                acc_ref[q, rows, :] = accs[q]
        for q in range(spec):
            y = jnp.sum(acc_ref[q].T, axis=0, keepdims=True)
            out_ref[q:q + 1, rr * BLOCK:(rr + 1) * BLOCK] = y
    width = out_ref.shape[1]
    lane = lax.broadcasted_iota(jnp.int32, (1, width), 1) + g * width
    tag = jnp.zeros((1, width), jnp.float32)
    for i in range(reg_ref.shape[0]):
        tag = jnp.where(lane == i, reg_ref[i].astype(jnp.float32), tag)
    out_ref[spec:spec + 1, :] = tag


def transport(left, mid, right, blocks, row_ptr, col_idx, regime):
    spec, cells = mid.shape
    slots = blocks.shape[0]
    nrows = row_ptr.shape[0] - 1
    groups = nrows // ROWS_PER_STEP
    window = ROWS_PER_STEP * KMAX
    whole = lambda g, rp, ci, rg: (0, 0)
    grid_spec = pltpu.PrefetchScalarGridSpec(
        num_scalar_prefetch=3,
        grid=(groups,),
        in_specs=[
            pl.BlockSpec(left.shape, whole),
            pl.BlockSpec(mid.shape, whole),
            pl.BlockSpec(right.shape, whole),
            pl.BlockSpec(
                (pl.Element(window), pl.Element(BLOCK), pl.Element(BLOCK)),
                lambda g, rp, ci, rg: (jnp.minimum(rp[g * ROWS_PER_STEP], slots - window), 0, 0),
            ),
        ],
        out_specs=pl.BlockSpec((spec + 1, ROWS_PER_STEP * BLOCK), lambda g, rp, ci, rg: (0, g)),
        scratch_shapes=[pltpu.VMEM((spec, BLOCK, BLOCK), jnp.float32)],
    )
    flops = 2 * slots * BLOCK * BLOCK * spec
    return pl.pallas_call(
        transport_kernel,
        grid_spec=grid_spec,
        out_shape=jax.ShapeDtypeStruct((spec + 1, nrows * BLOCK), jnp.float32),
        cost_estimate=pl.CostEstimate(
            flops=flops, bytes_accessed=blocks.size * 4 + 4 * mid.size * 4, transcendentals=0
        ),
    )(row_ptr, col_idx, regime, left, mid, right, blocks)


def chemistry_local(moved, block_jac):
    spec, cells = moved.shape
    nblk = cells // BLOCK
    per_block = moved.reshape(spec, nblk, BLOCK)
    out = jnp.einsum("but,ubc->tbc", block_jac, per_block, precision=lax.Precision.HIGHEST)
    return out.reshape(spec, cells)


def slot_kernel(rp_ref, col_ref, left_ref, mid_ref, right_ref, blk_ref, out_ref):
    g = pl.program_id(0)
    spec = out_ref.shape[2]
    nb_dev = mid_ref.shape[1] // BLOCK
    nb_total = nb_dev * lax.axis_size("cells")
    first = (lax.axis_index("cells") - 1) * nb_dev
    window = blk_ref.shape[0]
    slots = col_ref.shape[0]
    base = jnp.minimum(rp_ref[g * ROWS_PER_STEP], slots - window)
    for rr in range(ROWS_PER_STEP):
        r = g * ROWS_PER_STEP + rr
        start = rp_ref[r]
        cnt = rp_ref[r + 1] - start
        off = start - base
        for k in range(KMAX):
            local = jnp.clip(off + k, 0, window - 1)
            col = lax.rem(col_ref[base + local] - first + 2 * nb_total, nb_total)
            col = jnp.clip(col, 0, 3 * nb_dev - 1)
            piece = col // nb_dev
            lane = pl.multiple_of((col - piece * nb_dev) * BLOCK, BLOCK)
            x = jnp.where(
                piece == 0,
                left_ref[0:spec, pl.ds(lane, BLOCK)],
                jnp.where(piece == 1, mid_ref[0:spec, pl.ds(lane, BLOCK)], right_ref[0:spec, pl.ds(lane, BLOCK)]),
            )
            x = jnp.where(k < cnt, x, jnp.zeros_like(x))
            out_ref[rr, k] = lax.dot_general(
                x, blk_ref[local], (((1,), (1,)), ((), ())),
                precision=lax.Precision.HIGHEST, preferred_element_type=jnp.float32,
            )


def transport_slots(left, mid, right, blocks, row_ptr, col_idx):
    spec = mid.shape[0] - 1
    slots = blocks.shape[0]
    nrows = row_ptr.shape[0] - 1
    groups = nrows // ROWS_PER_STEP
    window = ROWS_PER_STEP * KMAX
    whole = lambda g, rp, ci: (0, 0)
    grid_spec = pltpu.PrefetchScalarGridSpec(
        num_scalar_prefetch=2,
        grid=(groups,),
        in_specs=[
            pl.BlockSpec(mid.shape, whole),
            pl.BlockSpec(mid.shape, whole),
            pl.BlockSpec(mid.shape, whole),
            pl.BlockSpec(
                (pl.Element(window), pl.Element(BLOCK), pl.Element(BLOCK)),
                lambda g, rp, ci: (jnp.minimum(rp[g * ROWS_PER_STEP], slots - window), 0, 0),
            ),
        ],
        out_specs=pl.BlockSpec((ROWS_PER_STEP, KMAX, spec, BLOCK), lambda g, rp, ci: (g, 0, 0, 0)),
    )
    return pl.pallas_call(
        slot_kernel,
        grid_spec=grid_spec,
        out_shape=jax.ShapeDtypeStruct((nrows, KMAX, spec, BLOCK), jnp.float32),
        cost_estimate=pl.CostEstimate(
            flops=2 * slots * BLOCK * BLOCK * spec, bytes_accessed=blocks.size * 4, transcendentals=0
        ),
    )(row_ptr, col_idx, left, mid, right, blocks)


def combine_kernel(rp_ref, col_ref, reg_ref, jac_ref, out_ref):
    own_rows = out_ref.shape[0]
    slots = col_ref.shape[0]
    nb_dev = reg_ref.shape[0] // 3
    nb_total = nb_dev * lax.axis_size("cells")
    first = (lax.axis_index("cells") - 1) * nb_dev
    for g in range(own_rows):
        row = lax.axis_index("tracer") * own_rows + g
        nreg = jac_ref.shape[0]
        row_jac = jac_ref[jnp.clip(reg_ref[nb_dev + row], 0, nreg - 1)]
        for k in range(KMAX):
            slot = jnp.minimum(rp_ref[row] + k, slots - 1)
            col = lax.rem(col_ref[slot] - first + 2 * nb_total, nb_total)
            col = jnp.clip(col, 0, 3 * nb_dev - 1)
            out_ref[g, k] = jnp.dot(
                jac_ref[jnp.clip(reg_ref[col], 0, nreg - 1)], row_jac,
                precision=lax.Precision.HIGHEST, preferred_element_type=jnp.float32,
            )


def combined_jac(row_ptr, col_idx, regime_ext, jac, own_rows):
    nreg, spec, _ = jac.shape
    grid_spec = pltpu.PrefetchScalarGridSpec(
        num_scalar_prefetch=3,
        grid=(1,),
        in_specs=[pl.BlockSpec(jac.shape, lambda i, rp, ci, rg: (0, 0, 0))],
        out_specs=pl.BlockSpec((own_rows, KMAX, spec, spec), lambda i, rp, ci, rg: (0, 0, 0, 0)),
    )
    return pl.pallas_call(
        combine_kernel,
        grid_spec=grid_spec,
        out_shape=jax.ShapeDtypeStruct((own_rows, KMAX, spec, spec), jnp.float32),
    )(row_ptr, col_idx, regime_ext, jac)


def halo(field):
    count = lax.axis_size("cells")
    left = lax.ppermute(field, "cells", [(i, (i + 1) % count) for i in range(count)])
    right = lax.ppermute(field, "cells", [((i + 1) % count, i) for i in range(count)])
    return left, right


def body(adjoint, blocks, row_ptr, col_idx, regime, jac):
    spec_dev, cells_dev = adjoint.shape
    nb_dev = cells_dev // BLOCK
    nb_total = nb_dev * lax.axis_size("cells")
    cell_index = lax.axis_index("cells")
    tracer_devices = lax.axis_size("tracer")
    tracer_index = lax.axis_index("tracer")
    pointers = row_ptr.reshape(-1)
    own_rows = nb_dev // tracer_devices
    left, right = halo(adjoint)
    moved = transport(left, adjoint, right, blocks, pointers, col_idx, regime)
    left, right = halo(moved)
    per_slot = transport_slots(left, moved, right, blocks, pointers, col_idx)
    regime_ext = jnp.concatenate(
        [left[spec_dev, :nb_dev], moved[spec_dev, :nb_dev], right[spec_dev, :nb_dev]]
    ).astype(jnp.int32)
    split = lax.all_to_all(per_slot, "tracer", 0, 2, tiled=True)
    combined = combined_jac(pointers, col_idx, regime_ext, jac, own_rows)
    reacted = jnp.einsum("gkvt,gkvc->tgc", combined, split, precision=lax.Precision.HIGHEST)
    reacted = reacted.reshape(reacted.shape[0], own_rows * BLOCK)
    return lax.all_to_all(reacted, "tracer", 0, 1, tiled=True)


def solution(mesh):
    return jax.shard_map(
        body,
        mesh=mesh,
        in_specs=(
            P("tracer", "cells"),
            P("cells", None, None),
            P("cells", None),
            P("cells"),
            P("cells"),
            P(),
        ),
        out_specs=P("tracer", "cells"),
        check_vma=False,
    )
```

```python
import jax
import jax.numpy as jnp
from jax import lax
from jax.experimental import pallas as pl
from jax.experimental.pallas import tpu as pltpu
from jax.sharding import PartitionSpec as P

BLOCK = 128
STEPS = 2
ROWS_PER_STEP = 4
KMAX = 4


def transport_kernel(rp_ref, col_ref, reg_ref, left_ref, mid_ref, right_ref, blk_ref, out_ref, acc_ref):
    g = pl.program_id(0)
    spec, cells = mid_ref.shape
    nb_dev = cells // BLOCK
    nb_total = nb_dev * lax.axis_size("cells")
    first = (lax.axis_index("cells") - 1) * nb_dev
    window = blk_ref.shape[0]
    slots = col_ref.shape[0]
    base = jnp.minimum(rp_ref[g * ROWS_PER_STEP], slots - window)
    for rr in range(ROWS_PER_STEP):
        r = g * ROWS_PER_STEP + rr
        start = rp_ref[r]
        cnt = rp_ref[r + 1] - start
        off = start - base
        xs = []
        for k in range(KMAX):
            local = jnp.clip(off + k, 0, window - 1)
            col = lax.rem(col_ref[base + local] - first + 2 * nb_total, nb_total)
            col = jnp.clip(col, 0, 3 * nb_dev - 1)
            piece = col // nb_dev
            lane = pl.multiple_of((col - piece * nb_dev) * BLOCK, BLOCK)
            x = jnp.where(
                piece == 0,
                left_ref[0:spec, pl.ds(lane, BLOCK)],
                jnp.where(piece == 1, mid_ref[:, pl.ds(lane, BLOCK)], right_ref[0:spec, pl.ds(lane, BLOCK)]),
            )
            x = jnp.where(k < cnt, x, jnp.zeros_like(x))
            xs.append((local, x))
        for ic in range(BLOCK // 32):
            rows = slice(ic * 32, (ic + 1) * 32)
            accs = [None] * spec
            for local, x in xs:
                b = blk_ref[local, rows, :]
                for q in range(spec):
                    term = b * x[q:q + 1, :]
                    accs[q] = term if accs[q] is None else accs[q] + term
            for q in range(spec):
                acc_ref[q, rows, :] = accs[q]
        for q in range(spec):
            y = jnp.sum(acc_ref[q].T, axis=0, keepdims=True)
            out_ref[q:q + 1, rr * BLOCK:(rr + 1) * BLOCK] = y
    width = out_ref.shape[1]
    lane = lax.broadcasted_iota(jnp.int32, (1, width), 1) + g * width
    tag = jnp.zeros((1, width), jnp.float32)
    for i in range(reg_ref.shape[0]):
        tag = jnp.where(lane == i, reg_ref[i].astype(jnp.float32), tag)
    out_ref[spec:spec + 1, :] = tag


def transport(left, mid, right, blocks, row_ptr, col_idx, regime):
    spec, cells = mid.shape
    slots = blocks.shape[0]
    nrows = row_ptr.shape[0] - 1
    groups = nrows // ROWS_PER_STEP
    window = ROWS_PER_STEP * KMAX
    whole = lambda g, rp, ci, rg: (0, 0)
    grid_spec = pltpu.PrefetchScalarGridSpec(
        num_scalar_prefetch=3,
        grid=(groups,),
        in_specs=[
            pl.BlockSpec(left.shape, whole),
            pl.BlockSpec(mid.shape, whole),
            pl.BlockSpec(right.shape, whole),
            pl.BlockSpec(
                (pl.Element(window), pl.Element(BLOCK), pl.Element(BLOCK)),
                lambda g, rp, ci, rg: (jnp.minimum(rp[g * ROWS_PER_STEP], slots - window), 0, 0),
            ),
        ],
        out_specs=pl.BlockSpec((spec + 1, ROWS_PER_STEP * BLOCK), lambda g, rp, ci, rg: (0, g)),
        scratch_shapes=[pltpu.VMEM((spec, BLOCK, BLOCK), jnp.float32)],
    )
    flops = 2 * slots * BLOCK * BLOCK * spec
    return pl.pallas_call(
        transport_kernel,
        grid_spec=grid_spec,
        out_shape=jax.ShapeDtypeStruct((spec + 1, nrows * BLOCK), jnp.float32),
        cost_estimate=pl.CostEstimate(
            flops=flops, bytes_accessed=blocks.size * 4 + 4 * mid.size * 4, transcendentals=0
        ),
    )(row_ptr, col_idx, regime, left, mid, right, blocks)


def chemistry_local(moved, block_jac):
    spec, cells = moved.shape
    nblk = cells // BLOCK
    per_block = moved.reshape(spec, nblk, BLOCK)
    out = jnp.einsum("but,ubc->tbc", block_jac, per_block, precision=lax.Precision.HIGHEST)
    return out.reshape(spec, cells)


def slot_kernel(rp_ref, col_ref, left_ref, mid_ref, right_ref, blk_ref, out_ref):
    g = pl.program_id(0)
    spec = out_ref.shape[2]
    nb_dev = mid_ref.shape[1] // BLOCK
    nb_total = nb_dev * lax.axis_size("cells")
    first = (lax.axis_index("cells") - 1) * nb_dev
    window = blk_ref.shape[0]
    slots = col_ref.shape[0]
    base = jnp.minimum(rp_ref[g * ROWS_PER_STEP], slots - window)
    for rr in range(ROWS_PER_STEP):
        r = g * ROWS_PER_STEP + rr
        start = rp_ref[r]
        cnt = rp_ref[r + 1] - start
        off = start - base
        for k in range(KMAX):
            local = jnp.clip(off + k, 0, window - 1)
            col = lax.rem(col_ref[base + local] - first + 2 * nb_total, nb_total)
            col = jnp.clip(col, 0, 3 * nb_dev - 1)
            piece = col // nb_dev
            lane = pl.multiple_of((col - piece * nb_dev) * BLOCK, BLOCK)
            x = jnp.where(
                piece == 0,
                left_ref[0:spec, pl.ds(lane, BLOCK)],
                jnp.where(piece == 1, mid_ref[0:spec, pl.ds(lane, BLOCK)], right_ref[0:spec, pl.ds(lane, BLOCK)]),
            )
            x = jnp.where(k < cnt, x, jnp.zeros_like(x))
            out_ref[rr, k] = lax.dot_general(
                x, blk_ref[local], (((1,), (1,)), ((), ())),
                precision=lax.Precision.HIGH, preferred_element_type=jnp.float32,
            )


def transport_slots(left, mid, right, blocks, row_ptr, col_idx):
    spec = mid.shape[0] - 1
    slots = blocks.shape[0]
    nrows = row_ptr.shape[0] - 1
    groups = nrows // ROWS_PER_STEP
    window = ROWS_PER_STEP * KMAX
    whole = lambda g, rp, ci: (0, 0)
    grid_spec = pltpu.PrefetchScalarGridSpec(
        num_scalar_prefetch=2,
        grid=(groups,),
        in_specs=[
            pl.BlockSpec(mid.shape, whole),
            pl.BlockSpec(mid.shape, whole),
            pl.BlockSpec(mid.shape, whole),
            pl.BlockSpec(
                (pl.Element(window), pl.Element(BLOCK), pl.Element(BLOCK)),
                lambda g, rp, ci: (jnp.minimum(rp[g * ROWS_PER_STEP], slots - window), 0, 0),
            ),
        ],
        out_specs=pl.BlockSpec((ROWS_PER_STEP, KMAX, spec, BLOCK), lambda g, rp, ci: (g, 0, 0, 0)),
    )
    return pl.pallas_call(
        slot_kernel,
        grid_spec=grid_spec,
        out_shape=jax.ShapeDtypeStruct((nrows, KMAX, spec, BLOCK), jnp.float32),
        cost_estimate=pl.CostEstimate(
            flops=2 * slots * BLOCK * BLOCK * spec, bytes_accessed=blocks.size * 4, transcendentals=0
        ),
    )(row_ptr, col_idx, left, mid, right, blocks)


def combine_kernel(rp_ref, col_ref, reg_ref, jac_ref, out_ref):
    own_rows = out_ref.shape[0]
    slots = col_ref.shape[0]
    nb_dev = reg_ref.shape[0] // 3
    nb_total = nb_dev * lax.axis_size("cells")
    first = (lax.axis_index("cells") - 1) * nb_dev
    for g in range(own_rows):
        row = lax.axis_index("tracer") * own_rows + g
        nreg = jac_ref.shape[0]
        row_jac = jac_ref[jnp.clip(reg_ref[nb_dev + row], 0, nreg - 1)]
        for k in range(KMAX):
            slot = jnp.minimum(rp_ref[row] + k, slots - 1)
            col = lax.rem(col_ref[slot] - first + 2 * nb_total, nb_total)
            col = jnp.clip(col, 0, 3 * nb_dev - 1)
            out_ref[g, k] = jnp.dot(
                jac_ref[jnp.clip(reg_ref[col], 0, nreg - 1)], row_jac,
                precision=lax.Precision.HIGHEST, preferred_element_type=jnp.float32,
            )


def combined_jac(row_ptr, col_idx, regime_ext, jac, own_rows):
    nreg, spec, _ = jac.shape
    grid_spec = pltpu.PrefetchScalarGridSpec(
        num_scalar_prefetch=3,
        grid=(1,),
        in_specs=[pl.BlockSpec(jac.shape, lambda i, rp, ci, rg: (0, 0, 0))],
        out_specs=pl.BlockSpec((own_rows, KMAX, spec, spec), lambda i, rp, ci, rg: (0, 0, 0, 0)),
    )
    return pl.pallas_call(
        combine_kernel,
        grid_spec=grid_spec,
        out_shape=jax.ShapeDtypeStruct((own_rows, KMAX, spec, spec), jnp.float32),
    )(row_ptr, col_idx, regime_ext, jac)


def halo(field):
    count = lax.axis_size("cells")
    left = lax.ppermute(field, "cells", [(i, (i + 1) % count) for i in range(count)])
    right = lax.ppermute(field, "cells", [((i + 1) % count, i) for i in range(count)])
    return left, right


def body(adjoint, blocks, row_ptr, col_idx, regime, jac):
    spec_dev, cells_dev = adjoint.shape
    nb_dev = cells_dev // BLOCK
    nb_total = nb_dev * lax.axis_size("cells")
    cell_index = lax.axis_index("cells")
    tracer_devices = lax.axis_size("tracer")
    tracer_index = lax.axis_index("tracer")
    pointers = row_ptr.reshape(-1)
    own_rows = nb_dev // tracer_devices
    left, right = halo(adjoint)
    moved = transport(left, adjoint, right, blocks, pointers, col_idx, regime)
    left, right = halo(moved)
    per_slot = transport_slots(left, moved, right, blocks, pointers, col_idx)
    regime_ext = jnp.concatenate(
        [left[spec_dev, :nb_dev], moved[spec_dev, :nb_dev], right[spec_dev, :nb_dev]]
    ).astype(jnp.int32)
    split = lax.all_to_all(per_slot, "tracer", 0, 2, tiled=True)
    combined = combined_jac(pointers, col_idx, regime_ext, jac, own_rows)
    reacted = jnp.einsum("gkvt,gkvc->tgc", combined, split, precision=lax.Precision.HIGHEST)
    reacted = reacted.reshape(reacted.shape[0], own_rows * BLOCK)
    return lax.all_to_all(reacted, "tracer", 0, 1, tiled=True)


def solution(mesh):
    return jax.shard_map(
        body,
        mesh=mesh,
        in_specs=(
            P("tracer", "cells"),
            P("cells", None, None),
            P("cells", None),
            P("cells"),
            P("cells"),
            P(),
        ),
        out_specs=P("tracer", "cells"),
        check_vma=False,
    )
```

```python
import jax
import jax.numpy as jnp
from jax import lax
from jax.experimental import pallas as pl
from jax.experimental.pallas import tpu as pltpu
from jax.sharding import PartitionSpec as P

BLOCK = 128
STEPS = 2
ROWS_PER_STEP = 8
KMAX = 4


def transport_kernel(rp_ref, col_ref, reg_ref, left_ref, mid_ref, right_ref, blk_ref, out_ref, acc_ref):
    g = pl.program_id(0)
    spec, cells = mid_ref.shape
    nb_dev = cells // BLOCK
    nb_total = nb_dev * lax.axis_size("cells")
    first = (lax.axis_index("cells") - 1) * nb_dev
    window = blk_ref.shape[0]
    slots = col_ref.shape[0]
    base = jnp.minimum(rp_ref[g * ROWS_PER_STEP], slots - window)
    for rr in range(ROWS_PER_STEP):
        r = g * ROWS_PER_STEP + rr
        start = rp_ref[r]
        cnt = rp_ref[r + 1] - start
        off = start - base
        xs = []
        for k in range(KMAX):
            local = jnp.clip(off + k, 0, window - 1)
            col = lax.rem(col_ref[base + local] - first + 2 * nb_total, nb_total)
            col = jnp.clip(col, 0, 3 * nb_dev - 1)
            piece = col // nb_dev
            lane = pl.multiple_of((col - piece * nb_dev) * BLOCK, BLOCK)
            x = jnp.where(
                piece == 0,
                left_ref[0:spec, pl.ds(lane, BLOCK)],
                jnp.where(piece == 1, mid_ref[:, pl.ds(lane, BLOCK)], right_ref[0:spec, pl.ds(lane, BLOCK)]),
            )
            x = jnp.where(k < cnt, x, jnp.zeros_like(x))
            xs.append((local, x))
        for ic in range(BLOCK // 32):
            rows = slice(ic * 32, (ic + 1) * 32)
            accs = [None] * spec
            for local, x in xs:
                b = blk_ref[local, rows, :]
                for q in range(spec):
                    term = b * x[q:q + 1, :]
                    accs[q] = term if accs[q] is None else accs[q] + term
            for q in range(spec):
                acc_ref[q, rows, :] = accs[q]
        for q in range(spec):
            y = jnp.sum(acc_ref[q].T, axis=0, keepdims=True)
            out_ref[q:q + 1, rr * BLOCK:(rr + 1) * BLOCK] = y
    width = out_ref.shape[1]
    lane = lax.broadcasted_iota(jnp.int32, (1, width), 1) + g * width
    tag = jnp.zeros((1, width), jnp.float32)
    for i in range(reg_ref.shape[0]):
        tag = jnp.where(lane == i, reg_ref[i].astype(jnp.float32), tag)
    out_ref[spec:spec + 1, :] = tag


def transport(left, mid, right, blocks, row_ptr, col_idx, regime):
    spec, cells = mid.shape
    slots = blocks.shape[0]
    nrows = row_ptr.shape[0] - 1
    groups = nrows // ROWS_PER_STEP
    window = ROWS_PER_STEP * KMAX
    whole = lambda g, rp, ci, rg: (0, 0)
    grid_spec = pltpu.PrefetchScalarGridSpec(
        num_scalar_prefetch=3,
        grid=(groups,),
        in_specs=[
            pl.BlockSpec(left.shape, whole),
            pl.BlockSpec(mid.shape, whole),
            pl.BlockSpec(right.shape, whole),
            pl.BlockSpec(
                (pl.Element(window), pl.Element(BLOCK), pl.Element(BLOCK)),
                lambda g, rp, ci, rg: (jnp.minimum(rp[g * ROWS_PER_STEP], slots - window), 0, 0),
            ),
        ],
        out_specs=pl.BlockSpec((spec + 1, ROWS_PER_STEP * BLOCK), lambda g, rp, ci, rg: (0, g)),
        scratch_shapes=[pltpu.VMEM((spec, BLOCK, BLOCK), jnp.float32)],
    )
    flops = 2 * slots * BLOCK * BLOCK * spec
    return pl.pallas_call(
        transport_kernel,
        grid_spec=grid_spec,
        out_shape=jax.ShapeDtypeStruct((spec + 1, nrows * BLOCK), jnp.float32),
        cost_estimate=pl.CostEstimate(
            flops=flops, bytes_accessed=blocks.size * 4 + 4 * mid.size * 4, transcendentals=0
        ),
    )(row_ptr, col_idx, regime, left, mid, right, blocks)


def chemistry_local(moved, block_jac):
    spec, cells = moved.shape
    nblk = cells // BLOCK
    per_block = moved.reshape(spec, nblk, BLOCK)
    out = jnp.einsum("but,ubc->tbc", block_jac, per_block, precision=lax.Precision.HIGHEST)
    return out.reshape(spec, cells)


def slot_kernel(rp_ref, col_ref, left_ref, mid_ref, right_ref, blk_ref, out_ref):
    g = pl.program_id(0)
    spec = out_ref.shape[2]
    nb_dev = mid_ref.shape[1] // BLOCK
    nb_total = nb_dev * lax.axis_size("cells")
    first = (lax.axis_index("cells") - 1) * nb_dev
    window = blk_ref.shape[0]
    slots = col_ref.shape[0]
    base = jnp.minimum(rp_ref[g * ROWS_PER_STEP], slots - window)
    for rr in range(ROWS_PER_STEP):
        r = g * ROWS_PER_STEP + rr
        start = rp_ref[r]
        cnt = rp_ref[r + 1] - start
        off = start - base
        for k in range(KMAX):
            local = jnp.clip(off + k, 0, window - 1)
            col = lax.rem(col_ref[base + local] - first + 2 * nb_total, nb_total)
            col = jnp.clip(col, 0, 3 * nb_dev - 1)
            piece = col // nb_dev
            lane = pl.multiple_of((col - piece * nb_dev) * BLOCK, BLOCK)
            x = jnp.where(
                piece == 0,
                left_ref[0:spec, pl.ds(lane, BLOCK)],
                jnp.where(piece == 1, mid_ref[0:spec, pl.ds(lane, BLOCK)], right_ref[0:spec, pl.ds(lane, BLOCK)]),
            )
            x = jnp.where(k < cnt, x, jnp.zeros_like(x))
            out_ref[rr, k] = lax.dot_general(
                x, blk_ref[local], (((1,), (1,)), ((), ())),
                precision=lax.Precision.HIGH, preferred_element_type=jnp.float32,
            )


def transport_slots(left, mid, right, blocks, row_ptr, col_idx):
    spec = mid.shape[0] - 1
    slots = blocks.shape[0]
    nrows = row_ptr.shape[0] - 1
    groups = nrows // ROWS_PER_STEP
    window = ROWS_PER_STEP * KMAX
    whole = lambda g, rp, ci: (0, 0)
    grid_spec = pltpu.PrefetchScalarGridSpec(
        num_scalar_prefetch=2,
        grid=(groups,),
        in_specs=[
            pl.BlockSpec(mid.shape, whole),
            pl.BlockSpec(mid.shape, whole),
            pl.BlockSpec(mid.shape, whole),
            pl.BlockSpec(
                (pl.Element(window), pl.Element(BLOCK), pl.Element(BLOCK)),
                lambda g, rp, ci: (jnp.minimum(rp[g * ROWS_PER_STEP], slots - window), 0, 0),
            ),
        ],
        out_specs=pl.BlockSpec((ROWS_PER_STEP, KMAX, spec, BLOCK), lambda g, rp, ci: (g, 0, 0, 0)),
    )
    return pl.pallas_call(
        slot_kernel,
        grid_spec=grid_spec,
        out_shape=jax.ShapeDtypeStruct((nrows, KMAX, spec, BLOCK), jnp.float32),
        cost_estimate=pl.CostEstimate(
            flops=2 * slots * BLOCK * BLOCK * spec, bytes_accessed=blocks.size * 4, transcendentals=0
        ),
    )(row_ptr, col_idx, left, mid, right, blocks)


def combine_kernel(rp_ref, col_ref, reg_ref, jac_ref, out_ref):
    own_rows = out_ref.shape[0]
    slots = col_ref.shape[0]
    nb_dev = reg_ref.shape[0] // 3
    nb_total = nb_dev * lax.axis_size("cells")
    first = (lax.axis_index("cells") - 1) * nb_dev
    for g in range(own_rows):
        row = lax.axis_index("tracer") * own_rows + g
        nreg = jac_ref.shape[0]
        row_jac = jac_ref[jnp.clip(reg_ref[nb_dev + row], 0, nreg - 1)]
        for k in range(KMAX):
            slot = jnp.minimum(rp_ref[row] + k, slots - 1)
            col = lax.rem(col_ref[slot] - first + 2 * nb_total, nb_total)
            col = jnp.clip(col, 0, 3 * nb_dev - 1)
            out_ref[g, k] = jnp.dot(
                jac_ref[jnp.clip(reg_ref[col], 0, nreg - 1)], row_jac,
                precision=lax.Precision.HIGHEST, preferred_element_type=jnp.float32,
            )


def combined_jac(row_ptr, col_idx, regime_ext, jac, own_rows):
    nreg, spec, _ = jac.shape
    grid_spec = pltpu.PrefetchScalarGridSpec(
        num_scalar_prefetch=3,
        grid=(1,),
        in_specs=[pl.BlockSpec(jac.shape, lambda i, rp, ci, rg: (0, 0, 0))],
        out_specs=pl.BlockSpec((own_rows, KMAX, spec, spec), lambda i, rp, ci, rg: (0, 0, 0, 0)),
    )
    return pl.pallas_call(
        combine_kernel,
        grid_spec=grid_spec,
        out_shape=jax.ShapeDtypeStruct((own_rows, KMAX, spec, spec), jnp.float32),
    )(row_ptr, col_idx, regime_ext, jac)


def halo(field):
    count = lax.axis_size("cells")
    left = lax.ppermute(field, "cells", [(i, (i + 1) % count) for i in range(count)])
    right = lax.ppermute(field, "cells", [((i + 1) % count, i) for i in range(count)])
    return left, right


def body(adjoint, blocks, row_ptr, col_idx, regime, jac):
    spec_dev, cells_dev = adjoint.shape
    nb_dev = cells_dev // BLOCK
    nb_total = nb_dev * lax.axis_size("cells")
    cell_index = lax.axis_index("cells")
    tracer_devices = lax.axis_size("tracer")
    tracer_index = lax.axis_index("tracer")
    pointers = row_ptr.reshape(-1)
    own_rows = nb_dev // tracer_devices
    left, right = halo(adjoint)
    moved = transport(left, adjoint, right, blocks, pointers, col_idx, regime)
    left, right = halo(moved)
    per_slot = transport_slots(left, moved, right, blocks, pointers, col_idx)
    regime_ext = jnp.concatenate(
        [left[spec_dev, :nb_dev], moved[spec_dev, :nb_dev], right[spec_dev, :nb_dev]]
    ).astype(jnp.int32)
    split = lax.all_to_all(per_slot, "tracer", 0, 2, tiled=True)
    combined = combined_jac(pointers, col_idx, regime_ext, jac, own_rows)
    reacted = jnp.einsum("gkvt,gkvc->tgc", combined, split, precision=lax.Precision.HIGHEST)
    reacted = reacted.reshape(reacted.shape[0], own_rows * BLOCK)
    return lax.all_to_all(reacted, "tracer", 0, 1, tiled=True)


def solution(mesh):
    return jax.shard_map(
        body,
        mesh=mesh,
        in_specs=(
            P("tracer", "cells"),
            P("cells", None, None),
            P("cells", None),
            P("cells"),
            P("cells"),
            P(),
        ),
        out_specs=P("tracer", "cells"),
        check_vma=False,
    )
```
